256 devices in a mesh: fsdp: 32 (over y, x, z_hi), tp: 8 (over z_lo, core).
Axes of the slice: x: 4, y: 4, z: 8 (z_hi: 2, z_lo: 4; z = z_hi * 4 + z_lo), core: 2. Of those that a mesh axis runs over, the one named last changes fastest.
Arguments:
- tokens: bfloat16 [16384, 4096], P(('fsdp', 'tp')), may hold values from -6 to 6
- in_weight: bfloat16 [4096, 3, 4096], P('fsdp', None, 'tp'), may hold values from -0.09375 to 0.09375
- out_weight: bfloat16 [4096, 4096], P('fsdp', 'tp'), may hold values from -0.09375 to 0.09375
- short_taps: float32 [3, 3, 4096], P(None, None, 'tp'), may hold values from -3 to 3
- filter_taps: float32 [128, 4096], P(None, 'tp'), may hold values from -1.2 to 1.2
- decay_rate: float32 [4096], P('tp'), may hold values from 0.00390625 to 0.09375
- doc_lengths: int32 [64], replicated, may hold values from 1 to 2048, 16384 in all
Outputs:
- mixed_out: bfloat16 [16384, 4096], P(('fsdp', 'tp'))
The draws below stay inside these ranges and needn't reach their ends.
Inputs may be any that keep to these rules, and one draw needn't show every extreme that they name: `doc_lengths`: the documents of the window in order; they sum to 16384.
All inputs are finite; a program needn't handle non-finite values.
Results may differ from the reference program's by a relative error of at most 0.014.
Values may be sent and summed in bfloat16 or wider, within the bound.
No kernel may reach another device: no remote copies, remote signals or barrier semaphores. Data moves between devices by JAX's collectives and lax.ppermute only.
A program may use at most 64 MiB of HBM per device.

```python
import math
import jax
import jax.numpy as jnp
import numpy as np
from jax import lax

D = 4096
DW = 4096
FILT = 128
SLAB = 512
TOKENS = 16384
DOCS = 64
N_FSDP = 32


def level_of(key, extent, pieces, smallest, top_value):
    def one(position, parts):
        heights = jax.random.uniform(jax.random.fold_in(jax.random.fold_in(key, 6), position), (parts,), jnp.float32, smallest / len(pieces), top_value / len(pieces))
        return jnp.repeat(jnp.exp(heights), extent[position] // parts).reshape((-1,) + (1,) * (len(extent) - position - 1))

    factor_of = one(*pieces[0])
    for cut in pieces[1:]:
        factor_of = factor_of * one(*cut)
    return factor_of


def length_profile(count, total, bound, slope):
    loads = [(1 << 20) // math.isqrt(standing ** slope) + 1 for standing in range(2, count + 1)]
    rest, holding = total - bound - (count - 1), [1] * (count - 1)
    while rest > 0:
        free = [i for i in range(count - 1) if holding[i] < bound]
        whole, left = sum([loads[i] for i in free]), rest
        for i in free:
            addition = min(bound - holding[i], max(1, left * loads[i] // whole), rest)
            holding[i] = holding[i] + addition
            rest = rest - addition
    return np.array([bound] + holding)


def ragged(rng, count, total, bound, slope):
    if count == 2:
        one = jax.random.randint(rng, (), max(1, total - bound), min(bound, total - 1) + 1)
        return jnp.stack([one, total - one])
    sizes = jnp.asarray(length_profile(count, total, bound, slope), jnp.int32)
    pairs = (count - 1) // 2
    donor, sink = sizes[1:1 + 2 * pairs:2], sizes[2:2 + 2 * pairs:2]
    margin = jnp.minimum(donor - 1, bound - sink)
    shifted = jax.random.randint(jax.random.fold_in(rng, 1), (pairs,), 0, 1 << 20) % (margin + 1)
    sizes = sizes.at[1:1 + 2 * pairs:2].set(donor - shifted).at[2:2 + 2 * pairs:2].set(sink + shifted)
    return sizes[jax.random.permutation(jax.random.fold_in(rng, 2), count)]


def scatter_about(rng, dims, width, bound, pieces=(), held_as=jnp.bfloat16):
    factor_of = level_of(rng, dims, pieces, -0.22, 0.18) if pieces else 1.0
    entries = jax.random.normal(rng, dims, jnp.float32) * width * factor_of
    return jnp.minimum(jnp.maximum(entries, -bound), bound).astype(held_as)


def setup_inputs(seed: int = 0) -> dict:
    key_of = jax.random.split(jax.random.key(seed), 8)
    return {
        "tokens": scatter_about(key_of[0], (TOKENS, D), 1.0, 6.0, ((0, 256),)),
        "in_weight": scatter_about(key_of[1], (D, 3, DW), D ** -0.5, 0.09375, ((0, 32), (2, 8))),
        "out_weight": scatter_about(key_of[2], (D, DW), DW ** -0.5, 0.09375, ((0, 32), (1, 8))),
        "short_taps": scatter_about(key_of[3], (3, 3, DW), 0.6, 3.0, ((2, 8),), jnp.float32),
        "filter_taps": scatter_about(key_of[4], (FILT, DW), 0.2, 1.2, ((1, 8),), jnp.float32),
        "decay_rate": jnp.clip(jnp.exp(math.log(0.09375) - 3.1780538 * jax.random.uniform(key_of[5], (DW,), jnp.float32) ** level_of(key_of[5], (DW,), ((0, 8),), -0.2, 0.2)), 0.00390625, 0.09375),
        "doc_lengths": ragged(key_of[6], DOCS, TOKENS, 4 * SLAB, 2).astype(jnp.int32),
    }


def doc_position(points, lengths):
    starts = jnp.cumsum(lengths).astype(jnp.int32) - lengths
    begins = lax.optimization_barrier(jnp.max(jnp.where(starts[None, :] <= points[:, None], starts[None, :], 0), axis=1))
    return (points - begins).astype(jnp.int32)

def short_filter(extended, short_taps, positions, out_count):
    running = jnp.zeros((out_count,) + extended.shape[1:], jnp.float32)
    for tap_index in range(3):
        window = extended[2 - tap_index:2 - tap_index + out_count].astype(jnp.float32)
        inside = (positions >= tap_index)[:, None, None]
        running = running + jnp.where(inside, short_taps[tap_index][None] * window, jnp.float32(0.0))
    return running

def reference(tokens, in_weight, out_weight, short_taps, filter_taps, decay_rate, doc_lengths):
    widened = tokens.astype(jnp.float32)
    normed = (widened * lax.rsqrt(lax.optimization_barrier(jnp.mean(widened * widened, axis=1, keepdims=True)) + 1e-06)).astype(jnp.bfloat16)
    flat_in = in_weight.reshape(D, 3 * DW)
    blocks = normed.reshape(N_FSDP, SLAB, D)
    projected = lax.map(lambda block: jnp.dot(block, flat_in, preferred_element_type=jnp.float32).astype(jnp.bfloat16), blocks)
    projected = projected.reshape(TOKENS, 3, DW)
    points = jnp.arange(TOKENS, dtype=jnp.int32)
    positions = doc_position(points, doc_lengths)
    padded = jnp.concatenate([jnp.zeros((2, 3, DW), projected.dtype), projected], 0)
    short_out = short_filter(padded, short_taps, positions, TOKENS)
    kv_product = (short_out[:, 1] * short_out[:, 2]).astype(jnp.bfloat16)
    shaped = filter_taps * jnp.exp(-decay_rate[None, :] * jnp.arange(FILT, dtype=jnp.float32)[:, None])
    kv_padded = jnp.concatenate([jnp.zeros((FILT, DW), kv_product.dtype), kv_product], 0)

    def one_tap(tap_index, running):
        window = lax.dynamic_slice_in_dim(kv_padded, (FILT - tap_index).astype(jnp.int32), TOKENS, 0)
        weight_row = lax.dynamic_slice_in_dim(shaped, tap_index.astype(jnp.int32), 1, 0)
        inside = (positions >= tap_index)[:, None]
        return running + jnp.where(inside, weight_row * window.astype(jnp.float32), jnp.float32(0.0))
    long_mix = lax.fori_loop(0, FILT, one_tap, jnp.zeros((TOKENS, DW), jnp.float32))
    gated_mix = (short_out[:, 0] * long_mix).astype(jnp.bfloat16)
    outgoing = lax.dot_general(gated_mix, out_weight, (((1,), (1,)), ((), ())), preferred_element_type=jnp.float32)
    return (widened + outgoing).astype(jnp.bfloat16)
```

```python
import jax
import jax.numpy as jnp
from jax import lax
from jax.sharding import Mesh
from jax.sharding import PartitionSpec as P

COL = ("zh", "zl", "c")


def doc_position(points, lengths):
    starts = jnp.cumsum(lengths) - lengths
    begins = jnp.max(jnp.where(starts[None, :] <= points[:, None], starts[None, :], 0), axis=1)
    return points - begins


def short_filter(extended, short_taps, positions, out_count):
    running = jnp.zeros((out_count,) + extended.shape[1:], jnp.float32)
    for tap_index in range(3):
        window = extended[2 - tap_index : 2 - tap_index + out_count].astype(jnp.float32)
        inside = (positions >= tap_index)[:, None, None]
        running = running + jnp.where(
            inside, short_taps[tap_index][None] * window, jnp.float32(0.0)
        )
    return running


def long_filter(extended, shaped, positions, out_count, tap_count):

    def tap_group(group_index, running):
        for inner in range(16):
            tap_index = group_index * 16 + inner
            window = lax.dynamic_slice_in_dim(extended, tap_count - tap_index, out_count, 0)
            weight_row = lax.dynamic_slice_in_dim(shaped, tap_index, 1, 0)
            inside = (positions >= tap_index)[:, None]
            running = running + jnp.where(
                inside, weight_row * window.astype(jnp.float32), jnp.float32(0.0)
            )
        return running

    zero_sum = jnp.zeros((out_count, shaped.shape[1]), jnp.float32)
    return lax.fori_loop(0, tap_count // 16, tap_group, zero_sum)


def swap_half(piece, zh, axis):
    width = piece.shape[axis] // 2
    lo = lax.slice_in_dim(piece, 0, width, axis=axis)
    hi = lax.slice_in_dim(piece, width, 2 * width, axis=axis)
    keep = jnp.where(zh == 0, lo, hi)
    give = jnp.where(zh == 0, hi, lo)
    got = lax.ppermute(give, "zh", [(0, 1), (1, 0)])
    first = jnp.where(zh == 0, keep, got)
    second = jnp.where(zh == 0, got, keep)
    return jnp.concatenate([first, second], 0)


def body(tokens, in_weight, out_weight, short_taps, filter_taps, decay_rate, doc_lengths):
    zh = lax.axis_index("zh")
    col_size = lax.axis_size("zh") * lax.axis_size("zl") * lax.axis_size("c")
    own_rows = tokens.shape[0]
    col_rows = own_rows * col_size
    half = in_weight.shape[2] // 2
    tap_count = filter_taps.shape[0]

    widened = tokens.astype(jnp.float32)
    normed = (
        widened * lax.rsqrt(jnp.mean(widened * widened, axis=1, keepdims=True) + 1e-06)
    ).astype(jnp.bfloat16)
    gathered = lax.all_gather(normed, COL, axis=0, tiled=True)

    in_piece = swap_half(in_weight, zh, 2)
    in_full = lax.all_gather(in_piece, "p", axis=0, tiled=True)
    out_piece = swap_half(out_weight, zh, 1)
    out_full = lax.all_gather(out_piece, "p", axis=0, tiled=True)

    flat_in = in_full.reshape(in_full.shape[0], 3 * half)
    projected = jnp.dot(gathered, flat_in, preferred_element_type=jnp.float32)
    projected = projected.astype(jnp.bfloat16).reshape(col_rows, 3, half)

    first_row = lax.axis_index("p") * col_rows
    own_points = first_row + jnp.arange(col_rows, dtype=jnp.int32)
    own_position = doc_position(own_points, doc_lengths)

    columns = lax.axis_size("p")
    ahead = [(i, i + 1) for i in range(columns - 1)]
    my_taps = lax.dynamic_slice_in_dim(short_taps, zh * half, half, 2)
    my_filter = lax.dynamic_slice_in_dim(filter_taps, zh * half, half, 1)
    my_decay = lax.dynamic_slice_in_dim(decay_rate, zh * half, half, 0)

    edge_rows = lax.ppermute(projected[col_rows - 2 :], "p", ahead)
    short_all = short_filter(
        jnp.concatenate([edge_rows, projected], 0), my_taps, own_position, col_rows
    )
    kv_product = (short_all[:, 1] * short_all[:, 2]).astype(jnp.bfloat16)
    tail_rows = lax.ppermute(kv_product[col_rows - tap_count :], "p", ahead)
    extended = jnp.concatenate([tail_rows, kv_product], 0)
    query = short_all[:, 0]
    shaped = my_filter * jnp.exp(
        -my_decay[None, :] * jnp.arange(tap_count, dtype=jnp.float32)[:, None]
    )
    long_mix = long_filter(extended, shaped, own_position, col_rows, tap_count)
    gated_mix = (query * long_mix).astype(jnp.bfloat16)
    summed = lax.psum_scatter(
        lax.dot_general(
            gated_mix, out_full, (((1,), (1,)), ((), ())), preferred_element_type=jnp.float32
        ).astype(jnp.bfloat16),
        COL,
        scatter_dimension=0,
        tiled=True,
    ).astype(jnp.float32)
    return (widened + summed).astype(jnp.bfloat16)


def solution(mesh):
    fsdp, tp = mesh.shape["fsdp"], mesh.shape["tp"]
    grid = mesh.devices.reshape(fsdp // 2, 2, tp // 2, 2)
    fine = Mesh(grid, ("p", "zh", "zl", "c"))
    rows = ("p", "zh", "zl", "c")
    chan = ("zl", "c")
    in_specs = (
        P(rows, None),
        P(("p", "zh"), None, chan),
        P(("p", "zh"), chan),
        P(None, None, chan),
        P(None, chan),
        P(chan),
        P(),
    )
    out_specs = P(rows, None)
    return jax.shard_map(body, mesh=fine, in_specs=in_specs, out_specs=out_specs, check_vma=False)
```

```python
import jax
import jax.numpy as jnp
from jax import lax
from jax.sharding import Mesh
from jax.sharding import PartitionSpec as P

COL = ("zh", "zl", "c")


def doc_position(points, lengths):
    starts = jnp.cumsum(lengths) - lengths
    begins = jnp.max(jnp.where(starts[None, :] <= points[:, None], starts[None, :], 0), axis=1)
    return points - begins


def short_filter(extended, short_taps, positions, out_count):
    running = jnp.zeros((out_count,) + extended.shape[1:], jnp.float32)
    for tap_index in range(3):
        window = extended[2 - tap_index : 2 - tap_index + out_count].astype(jnp.float32)
        inside = (positions >= tap_index)[:, None, None]
        running = running + jnp.where(
            inside, short_taps[tap_index][None] * window, jnp.float32(0.0)
        )
    return running


def long_filter(extended, shaped, positions, out_count, tap_count):

    def tap_group(group_index, running):
        for inner in range(16):
            tap_index = group_index * 16 + inner
            window = lax.dynamic_slice_in_dim(extended, tap_count - tap_index, out_count, 0)
            weight_row = lax.dynamic_slice_in_dim(shaped, tap_index, 1, 0)
            inside = (positions >= tap_index)[:, None]
            running = running + jnp.where(
                inside, weight_row * window.astype(jnp.float32), jnp.float32(0.0)
            )
        return running

    zero_sum = jnp.zeros((out_count, shaped.shape[1]), jnp.float32)
    return lax.fori_loop(0, tap_count // 16, tap_group, zero_sum)


def swap_half(piece, zh, axis):
    width = piece.shape[axis] // 2
    lo = lax.slice_in_dim(piece, 0, width, axis=axis)
    hi = lax.slice_in_dim(piece, width, 2 * width, axis=axis)
    keep = jnp.where(zh == 0, lo, hi)
    give = jnp.where(zh == 0, hi, lo)
    got = lax.ppermute(give, "zh", [(0, 1), (1, 0)])
    first = jnp.where(zh == 0, keep, got)
    second = jnp.where(zh == 0, got, keep)
    return jnp.concatenate([first, second], 0)


def z_ring_gather(block):
    nz = lax.axis_size("zh") * lax.axis_size("zl")
    z = lax.axis_index("zh") * lax.axis_size("zl") + lax.axis_index("zl")
    right = [(i, (i + 1) % nz) for i in range(nz)]
    left = [(i, (i - 1) % nz) for i in range(nz)]
    by_offset = {0: block}
    going_right, going_left = block, block
    for step in range(1, nz // 2 + 1):
        going_right = lax.ppermute(going_right, ("zh", "zl"), right)
        by_offset[-step] = going_right
        if step < nz - step:
            going_left = lax.ppermute(going_left, ("zh", "zl"), left)
            by_offset[step] = going_left
    lowest = -(nz // 2)
    relative = jnp.stack([by_offset[lowest + i] for i in range(nz)], 0)
    pick = (jnp.arange(nz, dtype=jnp.int32) - z - lowest) % nz
    return jnp.take(relative, pick, axis=0)


def body(tokens, in_weight, out_weight, short_taps, filter_taps, decay_rate, doc_lengths):
    zh = lax.axis_index("zh")
    col_size = lax.axis_size("zh") * lax.axis_size("zl") * lax.axis_size("c")
    own_rows = tokens.shape[0]
    col_rows = own_rows * col_size
    half = in_weight.shape[2] // 2
    tap_count = filter_taps.shape[0]

    widened = tokens.astype(jnp.float32)
    normed = (
        widened * lax.rsqrt(jnp.mean(widened * widened, axis=1, keepdims=True) + 1e-06)
    ).astype(jnp.bfloat16)
    gathered = z_ring_gather(normed)

    in_piece = swap_half(in_weight, zh, 2)
    in_full = lax.all_gather(in_piece, "p", axis=0, tiled=True)
    out_piece = swap_half(out_weight, zh, 1)
    out_full = lax.all_gather(out_piece, "p", axis=0, tiled=True)

    flat_in = in_full.reshape(in_full.shape[0], 3 * half)
    nz = gathered.shape[0]

    def project(rows):
        flat = rows.reshape(nz * own_rows, rows.shape[2])
        out = jnp.dot(flat, flat_in, preferred_element_type=jnp.float32)
        return out.astype(jnp.bfloat16).reshape(nz, own_rows, 3 * half)

    partner_rows = lax.ppermute(gathered, "c", [(0, 1), (1, 0)])
    from_mine = project(gathered)
    from_partner = project(partner_rows)
    core = lax.axis_index("c")
    first = jnp.where(core == 0, from_mine, from_partner)
    second = jnp.where(core == 0, from_partner, from_mine)
    projected = jnp.stack([first, second], 1).reshape(col_rows, 3, half)

    first_row = lax.axis_index("p") * col_rows
    own_points = first_row + jnp.arange(col_rows, dtype=jnp.int32)
    own_position = doc_position(own_points, doc_lengths)

    columns = lax.axis_size("p")
    ahead = [(i, i + 1) for i in range(columns - 1)]
    my_taps = lax.dynamic_slice_in_dim(short_taps, zh * half, half, 2)
    my_filter = lax.dynamic_slice_in_dim(filter_taps, zh * half, half, 1)
    my_decay = lax.dynamic_slice_in_dim(decay_rate, zh * half, half, 0)

    edge_rows = lax.ppermute(projected[col_rows - 2 :], "p", ahead)
    short_all = short_filter(
        jnp.concatenate([edge_rows, projected], 0), my_taps, own_position, col_rows
    )
    kv_product = (short_all[:, 1] * short_all[:, 2]).astype(jnp.bfloat16)
    tail_rows = lax.ppermute(kv_product[col_rows - tap_count :], "p", ahead)
    extended = jnp.concatenate([tail_rows, kv_product], 0)
    query = short_all[:, 0]
    shaped = my_filter * jnp.exp(
        -my_decay[None, :] * jnp.arange(tap_count, dtype=jnp.float32)[:, None]
    )
    long_mix = long_filter(extended, shaped, own_position, col_rows, tap_count)
    gated_mix = (query * long_mix).astype(jnp.bfloat16)
    summed = lax.psum_scatter(
        lax.dot_general(
            gated_mix, out_full, (((1,), (1,)), ((), ())), preferred_element_type=jnp.float32
        ).astype(jnp.bfloat16),
        COL,
        scatter_dimension=0,
        tiled=True,
    ).astype(jnp.float32)
    return (widened + summed).astype(jnp.bfloat16)


def solution(mesh):
    fsdp, tp = mesh.shape["fsdp"], mesh.shape["tp"]
    grid = mesh.devices.reshape(fsdp // 2, 2, tp // 2, 2)
    fine = Mesh(grid, ("p", "zh", "zl", "c"))
    rows = ("p", "zh", "zl", "c")
    chan = ("zl", "c")
    in_specs = (
        P(rows, None),
        P(("p", "zh"), None, chan),
        P(("p", "zh"), chan),
        P(None, None, chan),
        P(None, chan),
        P(chan),
        P(),
    )
    out_specs = P(rows, None)
    return jax.shard_map(body, mesh=fine, in_specs=in_specs, out_specs=out_specs, check_vma=False)
```

```python
import jax
import jax.numpy as jnp
from jax import lax
from jax.sharding import Mesh
from jax.sharding import PartitionSpec as P


def doc_position(points, lengths):
    starts = jnp.cumsum(lengths) - lengths
    begins = jnp.max(jnp.where(starts[None, :] <= points[:, None], starts[None, :], 0), axis=1)
    return points - begins


def short_filter(extended, short_taps, positions, out_count):
    running = jnp.zeros((out_count,) + extended.shape[1:], jnp.float32)
    for tap_index in range(3):
        window = extended[2 - tap_index : 2 - tap_index + out_count].astype(jnp.float32)
        inside = (positions >= tap_index)[:, None, None]
        running = running + jnp.where(
            inside, short_taps[tap_index][None] * window, jnp.float32(0.0)
        )
    return running


def long_filter(extended, shaped, positions, out_count, tap_count):

    def tap_group(group_index, running):
        for inner in range(16):
            tap_index = group_index * 16 + inner
            window = lax.dynamic_slice_in_dim(extended, tap_count - tap_index, out_count, 0)
            weight_row = lax.dynamic_slice_in_dim(shaped, tap_index, 1, 0)
            inside = (positions >= tap_index)[:, None]
            running = running + jnp.where(
                inside, weight_row * window.astype(jnp.float32), jnp.float32(0.0)
            )
        return running

    zero_sum = jnp.zeros((out_count, shaped.shape[1]), jnp.float32)
    return lax.fori_loop(0, tap_count // 16, tap_group, zero_sum)


def swap_half(piece, zh, axis):
    width = piece.shape[axis] // 2
    lo = lax.slice_in_dim(piece, 0, width, axis=axis)
    hi = lax.slice_in_dim(piece, width, 2 * width, axis=axis)
    keep = jnp.where(zh == 0, lo, hi)
    give = jnp.where(zh == 0, hi, lo)
    got = lax.ppermute(give, "zh", [(0, 1), (1, 0)])
    first = jnp.where(zh == 0, keep, got)
    second = jnp.where(zh == 0, got, keep)
    return jnp.concatenate([first, second], 0)


def z_ring_gather(block):
    nz = lax.axis_size("zh") * lax.axis_size("zl")
    z = lax.axis_index("zh") * lax.axis_size("zl") + lax.axis_index("zl")
    right = [(i, (i + 1) % nz) for i in range(nz)]
    left = [(i, (i - 1) % nz) for i in range(nz)]
    by_offset = {0: block}
    going_right, going_left = block, block
    for step in range(1, nz // 2 + 1):
        going_right = lax.ppermute(going_right, ("zh", "zl"), right)
        by_offset[-step] = going_right
        if step < nz - step:
            going_left = lax.ppermute(going_left, ("zh", "zl"), left)
            by_offset[step] = going_left
    lowest = -(nz // 2)
    relative = jnp.stack([by_offset[lowest + i] for i in range(nz)], 0)
    pick = (jnp.arange(nz, dtype=jnp.int32) - z - lowest) % nz
    return jnp.take(relative, pick, axis=0)


def block_body(tokens, in_weight, out_weight, short_taps, filter_taps, decay_rate, doc_lengths):
    zh = lax.axis_index("zh")
    col_size = lax.axis_size("zh") * lax.axis_size("zl") * lax.axis_size("c")
    own_rows = tokens.shape[0]
    col_rows = own_rows * col_size
    half = in_weight.shape[2] // 2
    tap_count = filter_taps.shape[0]

    widened = tokens.astype(jnp.float32)
    normed = (
        widened * lax.rsqrt(jnp.mean(widened * widened, axis=1, keepdims=True) + 1e-06)
    ).astype(jnp.bfloat16)
    in_piece = swap_half(in_weight, zh, 2)
    in_full = lax.all_gather(in_piece, "p", axis=0, tiled=True)
    gathered = z_ring_gather(normed)

    out_piece = swap_half(out_weight, zh, 1)
    out_full = lax.all_gather(out_piece, "p", axis=0, tiled=True)

    flat_in = in_full.reshape(in_full.shape[0], 3 * half)
    nz = gathered.shape[0]

    def project(rows):
        flat = rows.reshape(nz * own_rows, rows.shape[2])
        out = jnp.dot(flat, flat_in, preferred_element_type=jnp.float32)
        return out.astype(jnp.bfloat16).reshape(nz, own_rows, 3 * half)

    partner_rows = lax.ppermute(gathered, "c", [(0, 1), (1, 0)])
    from_mine = project(gathered)
    from_partner = project(partner_rows)
    core = lax.axis_index("c")
    first = jnp.where(core == 0, from_mine, from_partner)
    second = jnp.where(core == 0, from_partner, from_mine)
    projected = jnp.stack([first, second], 1).reshape(col_rows, 3, half)

    first_row = lax.axis_index("p") * col_rows
    own_points = first_row + jnp.arange(col_rows, dtype=jnp.int32)
    own_position = doc_position(own_points, doc_lengths)

    columns = lax.axis_size("p")
    ahead = [(i, i + 1) for i in range(columns - 1)]
    my_taps = lax.dynamic_slice_in_dim(short_taps, zh * half, half, 2)
    my_filter = lax.dynamic_slice_in_dim(filter_taps, zh * half, half, 1)
    my_decay = lax.dynamic_slice_in_dim(decay_rate, zh * half, half, 0)

    edge_rows = lax.ppermute(projected[col_rows - 2 :], "p", ahead)
    short_all = short_filter(
        jnp.concatenate([edge_rows, projected], 0), my_taps, own_position, col_rows
    )
    kv_product = (short_all[:, 1] * short_all[:, 2]).astype(jnp.bfloat16)
    tail_rows = lax.ppermute(kv_product[col_rows - tap_count :], "p", ahead)
    extended = jnp.concatenate([tail_rows, kv_product], 0)
    query = short_all[:, 0]
    shaped = my_filter * jnp.exp(
        -my_decay[None, :] * jnp.arange(tap_count, dtype=jnp.float32)[:, None]
    )
    long_mix = long_filter(extended, shaped, own_position, col_rows, tap_count)
    gated_mix = (query * long_mix).astype(jnp.bfloat16)
    core = lax.axis_index("c")
    swap = [(0, 1), (1, 0)]
    by_core = gated_mix.reshape(nz, 2, own_rows, half)
    mine_rows = lax.dynamic_index_in_dim(by_core, core, 1, keepdims=False)
    other_rows = lax.dynamic_index_in_dim(by_core, 1 - core, 1, keepdims=False)
    partner_cols = lax.ppermute(other_rows, "c", swap)
    partner_out = lax.ppermute(out_full, "c", swap)
    lhs = jnp.concatenate([mine_rows, partner_cols], 2).reshape(nz * own_rows, 2 * half)
    rhs = jnp.concatenate([out_full, partner_out], 1)
    summed = lax.psum_scatter(
        lax.dot_general(
            lhs, rhs, (((1,), (1,)), ((), ())), preferred_element_type=jnp.float32
        ).astype(jnp.bfloat16),
        ("zh", "zl"),
        scatter_dimension=0,
        tiled=True,
    ).astype(jnp.float32)
    return (widened + summed).astype(jnp.bfloat16)


def solution(mesh):
    fsdp, tp = mesh.shape["fsdp"], mesh.shape["tp"]
    grid = mesh.devices.reshape(fsdp // 2, 2, tp // 2, 2)
    fine = Mesh(grid, ("p", "zh", "zl", "c"))
    rows = ("p", "zh", "zl", "c")
    chan = ("zl", "c")
    in_specs = (
        P(rows, None),
        P(("p", "zh"), None, chan),
        P(("p", "zh"), chan),
        P(None, None, chan),
        P(None, chan),
        P(chan),
        P(),
    )
    out_specs = P(rows, None)
    return jax.shard_map(block_body, mesh=fine, in_specs=in_specs, out_specs=out_specs, check_vma=False)
```

```python
import jax
import jax.numpy as jnp
from jax import lax
from jax.sharding import Mesh
from jax.sharding import PartitionSpec as P


def doc_position(points, lengths):
    starts = jnp.cumsum(lengths) - lengths
    begins = jnp.max(jnp.where(starts[None, :] <= points[:, None], starts[None, :], 0), axis=1)
    return points - begins


def short_filter(extended, short_taps, positions, out_count):
    running = jnp.zeros((out_count,) + extended.shape[1:], jnp.float32)
    for tap_index in range(3):
        window = extended[2 - tap_index : 2 - tap_index + out_count].astype(jnp.float32)
        inside = (positions >= tap_index)[:, None, None]
        running = running + jnp.where(
            inside, short_taps[tap_index][None] * window, jnp.float32(0.0)
        )
    return running


def long_filter(extended, shaped, positions, out_count, tap_count):

    def tap_group(group_index, running):
        for inner in range(16):
            tap_index = group_index * 16 + inner
            window = lax.dynamic_slice_in_dim(extended, tap_count - tap_index, out_count, 0)
            weight_row = lax.dynamic_slice_in_dim(shaped, tap_index, 1, 0)
            inside = (positions >= tap_index)[:, None]
            running = running + jnp.where(
                inside, weight_row * window.astype(jnp.float32), jnp.float32(0.0)
            )
        return running

    zero_sum = jnp.zeros((out_count, shaped.shape[1]), jnp.float32)
    return lax.fori_loop(0, tap_count // 16, tap_group, zero_sum)


def swap_half(piece, zh, axis):
    width = piece.shape[axis] // 2
    lo = lax.slice_in_dim(piece, 0, width, axis=axis)
    hi = lax.slice_in_dim(piece, width, 2 * width, axis=axis)
    keep = jnp.where(zh == 0, lo, hi)
    give = jnp.where(zh == 0, hi, lo)
    got = lax.ppermute(give, "zh", [(0, 1), (1, 0)])
    first = jnp.where(zh == 0, keep, got)
    second = jnp.where(zh == 0, got, keep)
    return jnp.concatenate([first, second], 0)


def z_ring_gather(block):
    nz = lax.axis_size("zh") * lax.axis_size("zl")
    z = lax.axis_index("zh") * lax.axis_size("zl") + lax.axis_index("zl")
    right = [(i, (i + 1) % nz) for i in range(nz)]
    left = [(i, (i - 1) % nz) for i in range(nz)]
    by_offset = {0: block}
    going_right, going_left = block, block
    for step in range(1, nz // 2 + 1):
        going_right = lax.ppermute(going_right, ("zh", "zl"), right)
        by_offset[-step] = going_right
        if step < nz - step:
            going_left = lax.ppermute(going_left, ("zh", "zl"), left)
            by_offset[step] = going_left
    lowest = -(nz // 2)
    relative = jnp.stack([by_offset[lowest + i] for i in range(nz)], 0)
    pick = (jnp.arange(nz, dtype=jnp.int32) - z - lowest) % nz
    return jnp.take(relative, pick, axis=0)


def block_body(tokens, in_weight, out_weight, short_taps, filter_taps, decay_rate, doc_lengths):
    zh = lax.axis_index("zh")
    col_size = lax.axis_size("zh") * lax.axis_size("zl") * lax.axis_size("c")
    own_rows = tokens.shape[0]
    col_rows = own_rows * col_size
    half = in_weight.shape[2] // 2
    tap_count = filter_taps.shape[0]

    widened = tokens.astype(jnp.float32)
    normed = (
        widened * lax.rsqrt(jnp.mean(widened * widened, axis=1, keepdims=True) + 1e-06)
    ).astype(jnp.bfloat16)
    in_piece = swap_half(in_weight, zh, 2)
    in_full = lax.all_gather(in_piece, "p", axis=0, tiled=True)
    gathered = z_ring_gather(normed)

    chip_out = jnp.stack([out_weight, lax.ppermute(out_weight, "c", [(0, 1), (1, 0)])], 1)
    out_piece = swap_half(chip_out, zh, 2)
    out_full = lax.all_gather(out_piece, "p", axis=0, tiled=True)
    out_full = out_full.reshape(out_full.shape[0], 2 * half)

    flat_in = in_full.reshape(in_full.shape[0], 3 * half)
    nz = gathered.shape[0]

    def project(rows):
        flat = rows.reshape(nz * own_rows, rows.shape[2])
        out = jnp.dot(flat, flat_in, preferred_element_type=jnp.float32)
        return out.astype(jnp.bfloat16).reshape(nz, own_rows, 3 * half)

    partner_rows = lax.ppermute(gathered, "c", [(0, 1), (1, 0)])
    from_mine = project(gathered)
    from_partner = project(partner_rows)
    core = lax.axis_index("c")
    first = jnp.where(core == 0, from_mine, from_partner)
    second = jnp.where(core == 0, from_partner, from_mine)
    projected = jnp.stack([first, second], 1).reshape(col_rows, 3, half)

    first_row = lax.axis_index("p") * col_rows
    own_points = first_row + jnp.arange(col_rows, dtype=jnp.int32)
    own_position = doc_position(own_points, doc_lengths)

    columns = lax.axis_size("p")
    ahead = [(i, i + 1) for i in range(columns - 1)]
    my_taps = lax.dynamic_slice_in_dim(short_taps, zh * half, half, 2)
    my_filter = lax.dynamic_slice_in_dim(filter_taps, zh * half, half, 1)
    my_decay = lax.dynamic_slice_in_dim(decay_rate, zh * half, half, 0)

    edge_rows = lax.ppermute(projected[col_rows - 2 :], "p", ahead)
    short_all = short_filter(
        jnp.concatenate([edge_rows, projected], 0), my_taps, own_position, col_rows
    )
    kv_product = (short_all[:, 1] * short_all[:, 2]).astype(jnp.bfloat16)
    tail_rows = lax.ppermute(kv_product[col_rows - tap_count :], "p", ahead)
    extended = jnp.concatenate([tail_rows, kv_product], 0)
    query = short_all[:, 0]
    shaped = my_filter * jnp.exp(
        -my_decay[None, :] * jnp.arange(tap_count, dtype=jnp.float32)[:, None]
    )
    long_mix = long_filter(extended, shaped, own_position, col_rows, tap_count)
    gated_mix = (query * long_mix).astype(jnp.bfloat16)
    gated_mix, out_full = lax.optimization_barrier((gated_mix, out_full))
    core = lax.axis_index("c")
    swap = [(0, 1), (1, 0)]
    by_core = gated_mix.reshape(nz, 2, own_rows, half)
    mine_rows = lax.dynamic_index_in_dim(by_core, core, 1, keepdims=False)
    other_rows = lax.dynamic_index_in_dim(by_core, 1 - core, 1, keepdims=False)
    partner_cols = lax.ppermute(other_rows, "c", swap)
    lhs = jnp.concatenate([mine_rows, partner_cols], 2).reshape(nz * own_rows, 2 * half)
    rhs = out_full
    summed = lax.psum_scatter(
        lax.dot_general(
            lhs, rhs, (((1,), (1,)), ((), ())), preferred_element_type=jnp.float32
        ).astype(jnp.bfloat16),
        ("zh", "zl"),
        scatter_dimension=0,
        tiled=True,
    ).astype(jnp.float32)
    return (widened + summed).astype(jnp.bfloat16)


def solution(mesh):
    fsdp, tp = mesh.shape["fsdp"], mesh.shape["tp"]
    grid = mesh.devices.reshape(fsdp // 2, 2, tp // 2, 2)
    fine = Mesh(grid, ("p", "zh", "zl", "c"))
    rows = ("p", "zh", "zl", "c")
    chan = ("zl", "c")
    in_specs = (
        P(rows, None),
        P(("p", "zh"), None, chan),
        P(("p", "zh"), chan),
        P(None, None, chan),
        P(None, chan),
        P(chan),
        P(),
    )
    out_specs = P(rows, None)
    return jax.shard_map(block_body, mesh=fine, in_specs=in_specs, out_specs=out_specs, check_vma=False)
```

```python
import jax
import jax.numpy as jnp
from jax import lax
from jax.sharding import Mesh
from jax.sharding import PartitionSpec as P


def doc_position(points, lengths):
    starts = jnp.cumsum(lengths) - lengths
    begins = jnp.max(jnp.where(starts[None, :] <= points[:, None], starts[None, :], 0), axis=1)
    return points - begins


def short_filter(extended, short_taps, positions, out_count):
    running = jnp.zeros((out_count,) + extended.shape[1:], jnp.float32)
    for tap_index in range(3):
        window = extended[2 - tap_index : 2 - tap_index + out_count].astype(jnp.float32)
        inside = (positions >= tap_index)[:, None]
        running = running + jnp.where(
            inside, short_taps[tap_index][None] * window, jnp.float32(0.0)
        )
    return running


def long_filter(extended, shaped, positions, out_count, tap_count):

    def tap_group(group_index, running):
        for inner in range(16):
            tap_index = group_index * 16 + inner
            window = lax.dynamic_slice_in_dim(extended, tap_count - tap_index, out_count, 0)
            weight_row = lax.dynamic_slice_in_dim(shaped, tap_index, 1, 0)
            inside = (positions >= tap_index)[:, None]
            running = running + jnp.where(
                inside, weight_row * window.astype(jnp.float32), jnp.float32(0.0)
            )
        return running

    zero_sum = jnp.zeros((out_count, shaped.shape[1]), jnp.float32)
    return lax.fori_loop(0, tap_count // 16, tap_group, zero_sum)


def swap_half(piece, zh, axis):
    width = piece.shape[axis] // 2
    lo = lax.slice_in_dim(piece, 0, width, axis=axis)
    hi = lax.slice_in_dim(piece, width, 2 * width, axis=axis)
    keep = jnp.where(zh == 0, lo, hi)
    give = jnp.where(zh == 0, hi, lo)
    got = lax.ppermute(give, "zh", [(0, 1), (1, 0)])
    first = jnp.where(zh == 0, keep, got)
    second = jnp.where(zh == 0, got, keep)
    return jnp.concatenate([first, second], 0)


def z_ring_gather(block):
    nz = lax.axis_size("zh") * lax.axis_size("zl")
    z = lax.axis_index("zh") * lax.axis_size("zl") + lax.axis_index("zl")
    right = [(i, (i + 1) % nz) for i in range(nz)]
    left = [(i, (i - 1) % nz) for i in range(nz)]
    by_offset = {0: block}
    going_right, going_left = block, block
    for step in range(1, nz // 2 + 1):
        going_right = lax.ppermute(going_right, ("zh", "zl"), right)
        by_offset[-step] = going_right
        if step < nz - step:
            going_left = lax.ppermute(going_left, ("zh", "zl"), left)
            by_offset[step] = going_left
    lowest = -(nz // 2)
    relative = jnp.stack([by_offset[lowest + i] for i in range(nz)], 0)
    pick = (jnp.arange(nz, dtype=jnp.int32) - z - lowest) % nz
    return jnp.take(relative, pick, axis=0)


def block_body(tokens, in_weight, out_weight, short_taps, filter_taps, decay_rate, doc_lengths):
    zh = lax.axis_index("zh")
    col_size = lax.axis_size("zh") * lax.axis_size("zl") * lax.axis_size("c")
    own_rows = tokens.shape[0]
    col_rows = own_rows * col_size
    half = in_weight.shape[2] // 2
    tap_count = filter_taps.shape[0]

    widened = tokens.astype(jnp.float32)
    normed = (
        widened * lax.rsqrt(jnp.mean(widened * widened, axis=1, keepdims=True) + 1e-06)
    ).astype(jnp.bfloat16)
    in_piece = swap_half(in_weight, zh, 2)
    in_full = lax.all_gather(in_piece, "p", axis=0, tiled=True)
    gathered = z_ring_gather(normed)

    chip_out = jnp.stack([out_weight, lax.ppermute(out_weight, "c", [(0, 1), (1, 0)])], 1)
    out_piece = swap_half(chip_out, zh, 2)
    out_full = lax.all_gather(out_piece, "p", axis=0, tiled=True)
    out_full = out_full.reshape(out_full.shape[0], 2 * half)

    flat_in = in_full.reshape(in_full.shape[0], 3 * half)
    nz = gathered.shape[0]

    def project(rows):
        flat = rows.reshape(nz * own_rows, rows.shape[2])
        out = jnp.dot(flat, flat_in, preferred_element_type=jnp.float32)
        return out.astype(jnp.bfloat16).reshape(nz, own_rows, 3 * half)

    partner_rows = lax.ppermute(gathered, "c", [(0, 1), (1, 0)])
    from_mine = project(gathered)
    from_partner = project(partner_rows)
    core = lax.axis_index("c")
    first = jnp.where(core == 0, from_mine, from_partner)
    second = jnp.where(core == 0, from_partner, from_mine)
    projected = jnp.stack([first, second], 1).reshape(col_rows, 3 * half)

    first_row = lax.axis_index("p") * col_rows
    own_points = first_row + jnp.arange(col_rows, dtype=jnp.int32)
    own_position = doc_position(own_points, doc_lengths)

    columns = lax.axis_size("p")
    ahead = [(i, i + 1) for i in range(columns - 1)]
    my_taps = lax.dynamic_slice_in_dim(short_taps, zh * half, half, 2).reshape(3, 3 * half)
    my_filter = lax.dynamic_slice_in_dim(filter_taps, zh * half, half, 1)
    my_decay = lax.dynamic_slice_in_dim(decay_rate, zh * half, half, 0)

    edge_rows = lax.ppermute(projected[col_rows - 2 :], "p", ahead)
    short_all = short_filter(
        jnp.concatenate([edge_rows, projected], 0), my_taps, own_position, col_rows
    )
    kv_product = (short_all[:, half : 2 * half] * short_all[:, 2 * half :]).astype(jnp.bfloat16)
    tail_rows = lax.ppermute(kv_product[col_rows - tap_count :], "p", ahead)
    extended = jnp.concatenate([tail_rows, kv_product], 0)
    query = short_all[:, :half]
    shaped = my_filter * jnp.exp(
        -my_decay[None, :] * jnp.arange(tap_count, dtype=jnp.float32)[:, None]
    )
    long_mix = long_filter(extended, shaped, own_position, col_rows, tap_count)
    gated_mix = (query * long_mix).astype(jnp.bfloat16)
    gated_mix, out_full = lax.optimization_barrier((gated_mix, out_full))
    core = lax.axis_index("c")
    swap = [(0, 1), (1, 0)]
    by_core = gated_mix.reshape(nz, 2, own_rows, half)
    mine_rows = lax.dynamic_index_in_dim(by_core, core, 1, keepdims=False)
    other_rows = lax.dynamic_index_in_dim(by_core, 1 - core, 1, keepdims=False)
    partner_cols = lax.ppermute(other_rows, "c", swap)
    lhs = jnp.concatenate([mine_rows, partner_cols], 2).reshape(nz * own_rows, 2 * half)
    rhs = out_full
    summed = lax.psum_scatter(
        lax.dot_general(
            lhs, rhs, (((1,), (1,)), ((), ())), preferred_element_type=jnp.float32
        ).astype(jnp.bfloat16),
        ("zh", "zl"),
        scatter_dimension=0,
        tiled=True,
    ).astype(jnp.float32)
    return (widened + summed).astype(jnp.bfloat16)


def solution(mesh):
    fsdp, tp = mesh.shape["fsdp"], mesh.shape["tp"]
    grid = mesh.devices.reshape(fsdp // 2, 2, tp // 2, 2)
    fine = Mesh(grid, ("p", "zh", "zl", "c"))
    rows = ("p", "zh", "zl", "c")
    chan = ("zl", "c")
    in_specs = (
        P(rows, None),
        P(("p", "zh"), None, chan),
        P(("p", "zh"), chan),
        P(None, None, chan),
        P(None, chan),
        P(chan),
        P(),
    )
    out_specs = P(rows, None)
    return jax.shard_map(block_body, mesh=fine, in_specs=in_specs, out_specs=out_specs, check_vma=False)
```

```python
import jax
import jax.numpy as jnp
from jax import lax
from jax.sharding import Mesh
from jax.sharding import PartitionSpec as P


def doc_position(points, lengths):
    starts = jnp.cumsum(lengths) - lengths
    begins = jnp.max(jnp.where(starts[None, :] <= points[:, None], starts[None, :], 0), axis=1)
    return points - begins


def short_filter(extended, short_taps, positions, out_count):
    running = jnp.zeros((out_count,) + extended.shape[1:], jnp.float32)
    for tap_index in range(3):
        window = extended[2 - tap_index : 2 - tap_index + out_count].astype(jnp.float32)
        inside = (positions >= tap_index)[:, None]
        running = running + jnp.where(
            inside, short_taps[tap_index][None] * window, jnp.float32(0.0)
        )
    return running


def long_filter(extended, shaped, positions, blocks, part, parts, tap_count):
    out_count = positions.shape[0]
    block_rows = out_count // blocks
    sub = block_rows // parts
    pick = slice(part * sub, (part + 1) * sub)
    where_in = positions.reshape(blocks, block_rows)[:, pick]

    def tap_group(group_index, running):
        for inner in range(16):
            tap_index = group_index * 16 + inner
            window = lax.dynamic_slice_in_dim(extended, tap_count - tap_index, out_count, 0)
            window = window.reshape(blocks, block_rows, window.shape[1])[:, pick]
            weight_row = lax.dynamic_slice_in_dim(shaped, tap_index, 1, 0)
            inside = (where_in >= tap_index)[:, :, None]
            running = running + jnp.where(
                inside, weight_row[None] * window.astype(jnp.float32), jnp.float32(0.0)
            )
        return running

    zero_sum = jnp.zeros((blocks, sub, shaped.shape[1]), jnp.float32)
    return lax.fori_loop(0, tap_count // 16, tap_group, zero_sum)


def swap_half(piece, zh, axis):
    width = piece.shape[axis] // 2
    lo = lax.slice_in_dim(piece, 0, width, axis=axis)
    hi = lax.slice_in_dim(piece, width, 2 * width, axis=axis)
    keep = jnp.where(zh == 0, lo, hi)
    give = jnp.where(zh == 0, hi, lo)
    got = lax.ppermute(give, "zh", [(0, 1), (1, 0)])
    first = jnp.where(zh == 0, keep, got)
    second = jnp.where(zh == 0, got, keep)
    return jnp.concatenate([first, second], 0)


def z_ring_gather(block):
    nz = lax.axis_size("zh") * lax.axis_size("zl")
    z = lax.axis_index("zh") * lax.axis_size("zl") + lax.axis_index("zl")
    right = [(i, (i + 1) % nz) for i in range(nz)]
    left = [(i, (i - 1) % nz) for i in range(nz)]
    by_offset = {0: block}
    going_right, going_left = block, block
    for step in range(1, nz // 2 + 1):
        going_right = lax.ppermute(going_right, ("zh", "zl"), right)
        by_offset[-step] = going_right
        if step < nz - step:
            going_left = lax.ppermute(going_left, ("zh", "zl"), left)
            by_offset[step] = going_left
    lowest = -(nz // 2)
    relative = jnp.stack([by_offset[lowest + i] for i in range(nz)], 0)
    pick = (jnp.arange(nz, dtype=jnp.int32) - z - lowest) % nz
    return jnp.take(relative, pick, axis=0)


def block_body(tokens, in_weight, out_weight, short_taps, filter_taps, decay_rate, doc_lengths):
    zh = lax.axis_index("zh")
    col_size = lax.axis_size("zh") * lax.axis_size("zl") * lax.axis_size("c")
    own_rows = tokens.shape[0]
    col_rows = own_rows * col_size
    half = in_weight.shape[2] // 2
    tap_count = filter_taps.shape[0]

    widened = tokens.astype(jnp.float32)
    normed = (
        widened * lax.rsqrt(jnp.mean(widened * widened, axis=1, keepdims=True) + 1e-06)
    ).astype(jnp.bfloat16)
    in_piece = swap_half(in_weight, zh, 2)
    in_full = lax.all_gather(in_piece, "p", axis=0, tiled=True)
    gathered = z_ring_gather(normed)

    chip_out = jnp.stack([out_weight, lax.ppermute(out_weight, "c", [(0, 1), (1, 0)])], 1)
    out_piece = swap_half(chip_out, zh, 2)
    out_full = lax.all_gather(out_piece, "p", axis=0, tiled=True)
    out_full = out_full.reshape(out_full.shape[0], 2 * half)

    flat_in = in_full.reshape(in_full.shape[0], 3 * half)
    nz = gathered.shape[0]

    def project(rows):
        flat = rows.reshape(nz * own_rows, rows.shape[2])
        out = jnp.dot(flat, flat_in, preferred_element_type=jnp.float32)
        return out.astype(jnp.bfloat16).reshape(nz, own_rows, 3 * half)

    partner_rows = lax.ppermute(gathered, "c", [(0, 1), (1, 0)])
    from_mine = project(gathered)
    from_partner = project(partner_rows)
    core = lax.axis_index("c")
    first = jnp.where(core == 0, from_mine, from_partner)
    second = jnp.where(core == 0, from_partner, from_mine)
    projected = jnp.stack([first, second], 1).reshape(col_rows, 3 * half)

    first_row = lax.axis_index("p") * col_rows
    own_points = first_row + jnp.arange(col_rows, dtype=jnp.int32)
    own_position = doc_position(own_points, doc_lengths)

    columns = lax.axis_size("p")
    ahead = [(i, i + 1) for i in range(columns - 1)]
    my_taps = lax.dynamic_slice_in_dim(short_taps, zh * half, half, 2).reshape(3, 3 * half)
    my_filter = lax.dynamic_slice_in_dim(filter_taps, zh * half, half, 1)
    my_decay = lax.dynamic_slice_in_dim(decay_rate, zh * half, half, 0)

    edge_rows = lax.ppermute(projected[col_rows - 2 :], "p", ahead)
    short_all = short_filter(
        jnp.concatenate([edge_rows, projected], 0), my_taps, own_position, col_rows
    )
    kv_product = (short_all[:, half : 2 * half] * short_all[:, 2 * half :]).astype(jnp.bfloat16)
    tail_rows = lax.ppermute(kv_product[col_rows - tap_count :], "p", ahead)
    extended = jnp.concatenate([tail_rows, kv_product], 0)
    query = short_all[:, :half]
    shaped = my_filter * jnp.exp(
        -my_decay[None, :] * jnp.arange(tap_count, dtype=jnp.float32)[:, None]
    )
    core = lax.axis_index("c")
    swap = [(0, 1), (1, 0)]
    blocks = col_rows // own_rows
    parts = 2
    sub = own_rows // parts
    query_blocks = query.reshape(blocks, own_rows, half)
    pieces = []
    for part in range(parts):
        long_mix = long_filter(extended, shaped, own_position, blocks, part, parts, tap_count)
        gated_mix = (query_blocks[:, part * sub : (part + 1) * sub] * long_mix).astype(jnp.bfloat16)
        if part == 0:
            gated_mix, out_full = lax.optimization_barrier((gated_mix, out_full))
        by_core = gated_mix.reshape(nz, 2, sub, half)
        mine_rows = lax.dynamic_index_in_dim(by_core, core, 1, keepdims=False)
        other_rows = lax.dynamic_index_in_dim(by_core, 1 - core, 1, keepdims=False)
        partner_cols = lax.ppermute(other_rows, "c", swap)
        lhs = jnp.concatenate([mine_rows, partner_cols], 2).reshape(nz * sub, 2 * half)
        partial = lax.dot_general(
            lhs, out_full, (((1,), (1,)), ((), ())), preferred_element_type=jnp.float32
        ).astype(jnp.bfloat16)
        if part + 1 < parts:
            extended, partial = lax.optimization_barrier((extended, partial))
        pieces.append(lax.psum_scatter(partial, ("zh", "zl"), scatter_dimension=0, tiled=True))
    summed = jnp.concatenate(pieces, 0).astype(jnp.float32)
    return (widened + summed).astype(jnp.bfloat16)


def solution(mesh):
    fsdp, tp = mesh.shape["fsdp"], mesh.shape["tp"]
    grid = mesh.devices.reshape(fsdp // 2, 2, tp // 2, 2)
    fine = Mesh(grid, ("p", "zh", "zl", "c"))
    rows = ("p", "zh", "zl", "c")
    chan = ("zl", "c")
    in_specs = (
        P(rows, None),
        P(("p", "zh"), None, chan),
        P(("p", "zh"), chan),
        P(None, None, chan),
        P(None, chan),
        P(chan),
        P(),
    )
    out_specs = P(rows, None)
    return jax.shard_map(block_body, mesh=fine, in_specs=in_specs, out_specs=out_specs, check_vma=False)
```

```python
import jax
import jax.numpy as jnp
from jax import lax
from jax.sharding import Mesh
from jax.sharding import PartitionSpec as P


def doc_position(points, lengths):
    starts = jnp.cumsum(lengths) - lengths
    begins = jnp.max(jnp.where(starts[None, :] <= points[:, None], starts[None, :], 0), axis=1)
    return points - begins


def short_filter(extended, short_taps, positions, out_count):
    running = jnp.zeros((out_count,) + extended.shape[1:], jnp.float32)
    for tap_index in range(3):
        window = extended[2 - tap_index : 2 - tap_index + out_count].astype(jnp.float32)
        inside = (positions >= tap_index)[:, None]
        running = running + jnp.where(
            inside, short_taps[tap_index][None] * window, jnp.float32(0.0)
        )
    return running


def long_filter(extended, shaped, positions, out_count, tap_count):

    def tap_group(group_index, running):
        for inner in range(16):
            tap_index = group_index * 16 + inner
            window = lax.dynamic_slice_in_dim(extended, tap_count - tap_index, out_count, 0)
            weight_row = lax.dynamic_slice_in_dim(shaped, tap_index, 1, 0)
            inside = (positions >= tap_index)[:, None]
            running = running + jnp.where(
                inside, weight_row * window.astype(jnp.float32), jnp.float32(0.0)
            )
        return running

    zero_sum = jnp.zeros((out_count, shaped.shape[1]), jnp.float32)
    return lax.fori_loop(0, tap_count // 16, tap_group, zero_sum)


def swap_half(piece, zh, axis):
    width = piece.shape[axis] // 2
    lo = lax.slice_in_dim(piece, 0, width, axis=axis)
    hi = lax.slice_in_dim(piece, width, 2 * width, axis=axis)
    keep = jnp.where(zh == 0, lo, hi)
    give = jnp.where(zh == 0, hi, lo)
    got = lax.ppermute(give, "zh", [(0, 1), (1, 0)])
    first = jnp.where(zh == 0, keep, got)
    second = jnp.where(zh == 0, got, keep)
    return jnp.concatenate([first, second], 0)


def z_ring_gather(block):
    nz = lax.axis_size("zh") * lax.axis_size("zl")
    z = lax.axis_index("zh") * lax.axis_size("zl") + lax.axis_index("zl")
    right = [(i, (i + 1) % nz) for i in range(nz)]
    left = [(i, (i - 1) % nz) for i in range(nz)]
    by_offset = {0: block}
    going_right, going_left = block, block
    for step in range(1, nz // 2 + 1):
        going_right = lax.ppermute(going_right, ("zh", "zl"), right)
        by_offset[-step] = going_right
        if step < nz - step:
            going_left = lax.ppermute(going_left, ("zh", "zl"), left)
            by_offset[step] = going_left
    lowest = -(nz // 2)
    relative = jnp.stack([by_offset[lowest + i] for i in range(nz)], 0)
    pick = (jnp.arange(nz, dtype=jnp.int32) - z - lowest) % nz
    return relative, pick


def block_body(tokens, in_weight, out_weight, short_taps, filter_taps, decay_rate, doc_lengths):
    zh = lax.axis_index("zh")
    col_size = lax.axis_size("zh") * lax.axis_size("zl") * lax.axis_size("c")
    own_rows = tokens.shape[0]
    col_rows = own_rows * col_size
    half = in_weight.shape[2] // 2
    tap_count = filter_taps.shape[0]

    widened = tokens.astype(jnp.float32)
    normed = (
        widened * lax.rsqrt(jnp.mean(widened * widened, axis=1, keepdims=True) + 1e-06)
    ).astype(jnp.bfloat16)
    in_piece = swap_half(in_weight, zh, 2)
    in_full = lax.all_gather(in_piece, "p", axis=0, tiled=True)
    gathered, pick = z_ring_gather(normed)

    chip_out = jnp.stack([out_weight, lax.ppermute(out_weight, "c", [(0, 1), (1, 0)])], 1)
    out_piece = swap_half(chip_out, zh, 2)
    out_full = lax.all_gather(out_piece, "p", axis=0, tiled=True)
    out_full = out_full.reshape(out_full.shape[0], 2 * half)

    flat_in = in_full.reshape(in_full.shape[0], 3 * half)
    nz = gathered.shape[0]

    def project(rows):
        flat = rows.reshape(nz * own_rows, rows.shape[2])
        out = jnp.dot(flat, flat_in, preferred_element_type=jnp.float32)
        return out.astype(jnp.bfloat16).reshape(nz, own_rows, 3 * half)

    partner_rows = lax.ppermute(gathered, "c", [(0, 1), (1, 0)])
    from_mine = project(gathered)
    from_partner = project(partner_rows)
    core = lax.axis_index("c")
    both = jnp.concatenate([from_mine, from_partner], 0)
    from_core = jnp.array([[0, 1]], jnp.int32) != core
    order = (from_core.astype(jnp.int32) * nz + pick[:, None]).reshape(2 * nz)
    projected = jnp.take(both, order, axis=0).reshape(col_rows, 3 * half)

    first_row = lax.axis_index("p") * col_rows
    own_points = first_row + jnp.arange(col_rows, dtype=jnp.int32)
    own_position = doc_position(own_points, doc_lengths)

    columns = lax.axis_size("p")
    ahead = [(i, i + 1) for i in range(columns - 1)]
    my_taps = lax.dynamic_slice_in_dim(short_taps, zh * half, half, 2).reshape(3, 3 * half)
    my_filter = lax.dynamic_slice_in_dim(filter_taps, zh * half, half, 1)
    my_decay = lax.dynamic_slice_in_dim(decay_rate, zh * half, half, 0)

    edge_rows = lax.ppermute(projected[col_rows - 2 :], "p", ahead)
    short_all = short_filter(
        jnp.concatenate([edge_rows, projected], 0), my_taps, own_position, col_rows
    )
    kv_product = (short_all[:, half : 2 * half] * short_all[:, 2 * half :]).astype(jnp.bfloat16)
    tail_rows = lax.ppermute(kv_product[col_rows - tap_count :], "p", ahead)
    extended = jnp.concatenate([tail_rows, kv_product], 0)
    query = short_all[:, :half]
    shaped = my_filter * jnp.exp(
        -my_decay[None, :] * jnp.arange(tap_count, dtype=jnp.float32)[:, None]
    )
    long_mix = long_filter(extended, shaped, own_position, col_rows, tap_count)
    gated_mix = (query * long_mix).astype(jnp.bfloat16)
    gated_mix, out_full = lax.optimization_barrier((gated_mix, out_full))
    core = lax.axis_index("c")
    swap = [(0, 1), (1, 0)]
    by_core = gated_mix.reshape(nz, 2, own_rows, half)
    mine_rows = lax.dynamic_index_in_dim(by_core, core, 1, keepdims=False)
    other_rows = lax.dynamic_index_in_dim(by_core, 1 - core, 1, keepdims=False)
    partner_cols = lax.ppermute(other_rows, "c", swap)
    lhs = jnp.concatenate([mine_rows, partner_cols], 2).reshape(nz * own_rows, 2 * half)
    rhs = out_full
    summed = lax.psum_scatter(
        lax.dot_general(
            lhs, rhs, (((1,), (1,)), ((), ())), preferred_element_type=jnp.float32
        ).astype(jnp.bfloat16),
        ("zh", "zl"),
        scatter_dimension=0,
        tiled=True,
    ).astype(jnp.float32)
    return (widened + summed).astype(jnp.bfloat16)


def solution(mesh):
    fsdp, tp = mesh.shape["fsdp"], mesh.shape["tp"]
    grid = mesh.devices.reshape(fsdp // 2, 2, tp // 2, 2)
    fine = Mesh(grid, ("p", "zh", "zl", "c"))
    rows = ("p", "zh", "zl", "c")
    chan = ("zl", "c")
    in_specs = (
        P(rows, None),
        P(("p", "zh"), None, chan),
        P(("p", "zh"), chan),
        P(None, None, chan),
        P(None, chan),
        P(chan),
        P(),
    )
    out_specs = P(rows, None)
    return jax.shard_map(block_body, mesh=fine, in_specs=in_specs, out_specs=out_specs, check_vma=False)
```

```python
import jax
import jax.numpy as jnp
from jax import lax
from jax.sharding import Mesh
from jax.sharding import PartitionSpec as P


def doc_position(points, lengths):
    starts = jnp.cumsum(lengths) - lengths
    begins = jnp.max(jnp.where(starts[None, :] <= points[:, None], starts[None, :], 0), axis=1)
    return points - begins


def short_filter(extended, short_taps, positions, out_count):
    running = jnp.zeros((out_count,) + extended.shape[1:], jnp.float32)
    for tap_index in range(3):
        window = extended[2 - tap_index : 2 - tap_index + out_count].astype(jnp.float32)
        inside = (positions >= tap_index)[:, None]
        running = running + jnp.where(
            inside, short_taps[tap_index][None] * window, jnp.float32(0.0)
        )
    return running


def long_filter(extended, shaped, positions, out_count, tap_count):

    def tap_group(group_index, running):
        for inner in range(16):
            tap_index = group_index * 16 + inner
            window = lax.dynamic_slice_in_dim(extended, tap_count - tap_index, out_count, 0)
            weight_row = lax.dynamic_slice_in_dim(shaped, tap_index, 1, 0)
            inside = (positions >= tap_index)[:, None]
            running = running + jnp.where(
                inside, weight_row * window.astype(jnp.float32), jnp.float32(0.0)
            )
        return running

    zero_sum = jnp.zeros((out_count, shaped.shape[1]), jnp.float32)
    return lax.fori_loop(0, tap_count // 16, tap_group, zero_sum)


def swap_half(piece, zh, axis):
    width = piece.shape[axis] // 2
    lo = lax.slice_in_dim(piece, 0, width, axis=axis)
    hi = lax.slice_in_dim(piece, width, 2 * width, axis=axis)
    keep = jnp.where(zh == 0, lo, hi)
    give = jnp.where(zh == 0, hi, lo)
    got = lax.ppermute(give, "zh", [(0, 1), (1, 0)])
    first = jnp.where(zh == 0, keep, got)
    second = jnp.where(zh == 0, got, keep)
    return jnp.concatenate([first, second], 0)


def z_ring_gather(block):
    nz = lax.axis_size("zh") * lax.axis_size("zl")
    z = lax.axis_index("zh") * lax.axis_size("zl") + lax.axis_index("zl")
    right = [(i, (i + 1) % nz) for i in range(nz)]
    left = [(i, (i - 1) % nz) for i in range(nz)]
    by_offset = {0: block}
    going_right, going_left = block, block
    for step in range(1, nz // 2 + 1):
        going_right = lax.ppermute(going_right, ("zh", "zl"), right)
        by_offset[-step] = going_right
        if step < nz - step:
            going_left = lax.ppermute(going_left, ("zh", "zl"), left)
            by_offset[step] = going_left
    lowest = -(nz // 2)
    relative = jnp.stack([by_offset[lowest + i] for i in range(nz)], 0)
    pick = (jnp.arange(nz, dtype=jnp.int32) - z - lowest) % nz
    return relative, pick


def block_body(tokens, in_weight, out_weight, short_taps, filter_taps, decay_rate, doc_lengths):
    zh = lax.axis_index("zh")
    col_size = lax.axis_size("zh") * lax.axis_size("zl") * lax.axis_size("c")
    own_rows = tokens.shape[0]
    col_rows = own_rows * col_size
    half = in_weight.shape[2] // 2
    tap_count = filter_taps.shape[0]

    widened = tokens.astype(jnp.float32)
    normed = (
        widened * lax.rsqrt(jnp.mean(widened * widened, axis=1, keepdims=True) + 1e-06)
    ).astype(jnp.bfloat16)
    in_piece = swap_half(in_weight, zh, 2)
    in_full = lax.all_gather(in_piece, "p", axis=0, tiled=True)
    gathered, pick = z_ring_gather(normed)

    chip_out = jnp.stack([out_weight, lax.ppermute(out_weight, "c", [(0, 1), (1, 0)])], 1)
    out_piece = swap_half(chip_out, zh, 2)
    out_full = lax.all_gather(out_piece, "p", axis=0, tiled=True)
    out_full = out_full.reshape(out_full.shape[0], 2 * half)

    flat_in = in_full.reshape(in_full.shape[0], 3 * half)
    nz = gathered.shape[0]

    def project(rows):
        flat = rows.reshape(nz * own_rows, rows.shape[2])
        out = jnp.dot(flat, flat_in, preferred_element_type=jnp.float32)
        return out.astype(jnp.bfloat16).reshape(nz, own_rows, 3 * half)

    partner_rows = lax.ppermute(gathered, "c", [(0, 1), (1, 0)])
    from_mine = project(gathered)
    from_partner = project(partner_rows)
    core = lax.axis_index("c")
    both = jnp.concatenate([from_mine, from_partner], 0)
    from_core = jnp.array([[0, 1]], jnp.int32) != core
    order = (from_core.astype(jnp.int32) * nz + pick[:, None]).reshape(2 * nz)
    projected = jnp.take(both, order, axis=0).reshape(col_rows, 3 * half)

    first_row = lax.axis_index("p") * col_rows
    wide_rows = tap_count + col_rows
    wide_points = first_row - tap_count + jnp.arange(wide_rows, dtype=jnp.int32)
    wide_position = doc_position(wide_points, doc_lengths)
    own_position = wide_position[tap_count:]

    columns = lax.axis_size("p")
    ahead = [(i, i + 1) for i in range(columns - 1)]
    my_taps = lax.dynamic_slice_in_dim(short_taps, zh * half, half, 2).reshape(3, 3 * half)
    my_filter = lax.dynamic_slice_in_dim(filter_taps, zh * half, half, 1)
    my_decay = lax.dynamic_slice_in_dim(decay_rate, zh * half, half, 0)

    before = lax.ppermute(projected[col_rows - tap_count - 2 :], "p", ahead)
    short_all = short_filter(
        jnp.concatenate([before, projected], 0), my_taps, wide_position, wide_rows
    )
    extended = (short_all[:, half : 2 * half] * short_all[:, 2 * half :]).astype(jnp.bfloat16)
    query = short_all[tap_count:, :half]
    shaped = my_filter * jnp.exp(
        -my_decay[None, :] * jnp.arange(tap_count, dtype=jnp.float32)[:, None]
    )
    long_mix = long_filter(extended, shaped, own_position, col_rows, tap_count)
    gated_mix = (query * long_mix).astype(jnp.bfloat16)
    gated_mix, out_full = lax.optimization_barrier((gated_mix, out_full))
    core = lax.axis_index("c")
    swap = [(0, 1), (1, 0)]
    by_core = gated_mix.reshape(nz, 2, own_rows, half)
    mine_rows = lax.dynamic_index_in_dim(by_core, core, 1, keepdims=False)
    other_rows = lax.dynamic_index_in_dim(by_core, 1 - core, 1, keepdims=False)
    partner_cols = lax.ppermute(other_rows, "c", swap)
    lhs = jnp.concatenate([mine_rows, partner_cols], 2).reshape(nz * own_rows, 2 * half)
    rhs = out_full
    summed = lax.psum_scatter(
        lax.dot_general(
            lhs, rhs, (((1,), (1,)), ((), ())), preferred_element_type=jnp.float32
        ).astype(jnp.bfloat16),
        ("zh", "zl"),
        scatter_dimension=0,
        tiled=True,
    ).astype(jnp.float32)
    return (widened + summed).astype(jnp.bfloat16)


def solution(mesh):
    fsdp, tp = mesh.shape["fsdp"], mesh.shape["tp"]
    grid = mesh.devices.reshape(fsdp // 2, 2, tp // 2, 2)
    fine = Mesh(grid, ("p", "zh", "zl", "c"))
    rows = ("p", "zh", "zl", "c")
    chan = ("zl", "c")
    in_specs = (
        P(rows, None),
        P(("p", "zh"), None, chan),
        P(("p", "zh"), chan),
        P(None, None, chan),
        P(None, chan),
        P(chan),
        P(),
    )
    out_specs = P(rows, None)
    return jax.shard_map(block_body, mesh=fine, in_specs=in_specs, out_specs=out_specs, check_vma=False)
```

```python
import jax
import jax.numpy as jnp
from jax import lax
from jax.sharding import Mesh
from jax.sharding import PartitionSpec as P


def doc_position(points, lengths):
    starts = jnp.cumsum(lengths) - lengths
    begins = jnp.max(jnp.where(starts[None, :] <= points[:, None], starts[None, :], 0), axis=1)
    return points - begins


def short_filter(extended, short_taps, positions, out_count):
    running = jnp.zeros((out_count,) + extended.shape[1:], jnp.float32)
    for tap_index in range(3):
        window = extended[2 - tap_index : 2 - tap_index + out_count].astype(jnp.float32)
        inside = (positions >= tap_index)[:, None]
        running = running + jnp.where(
            inside, short_taps[tap_index][None] * window, jnp.float32(0.0)
        )
    return running


def long_filter(extended, shaped, positions, out_count, tap_count):

    def tap_group(group_index, running):
        for inner in range(16):
            tap_index = group_index * 16 + inner
            window = lax.dynamic_slice_in_dim(extended, tap_count - tap_index, out_count, 0)
            weight_row = lax.dynamic_slice_in_dim(shaped, tap_index, 1, 0)
            inside = (positions >= tap_index)[:, None]
            running = running + jnp.where(
                inside, weight_row * window.astype(jnp.float32), jnp.float32(0.0)
            )
        return running

    zero_sum = jnp.zeros((out_count, shaped.shape[1]), jnp.float32)
    return lax.fori_loop(0, tap_count // 16, tap_group, zero_sum, unroll=True)


def swap_half(piece, zh, axis):
    width = piece.shape[axis] // 2
    lo = lax.slice_in_dim(piece, 0, width, axis=axis)
    hi = lax.slice_in_dim(piece, width, 2 * width, axis=axis)
    keep = jnp.where(zh == 0, lo, hi)
    give = jnp.where(zh == 0, hi, lo)
    got = lax.ppermute(give, "zh", [(0, 1), (1, 0)])
    first = jnp.where(zh == 0, keep, got)
    second = jnp.where(zh == 0, got, keep)
    return jnp.concatenate([first, second], 0)


def z_ring_gather(block):
    nz = lax.axis_size("zh") * lax.axis_size("zl")
    z = lax.axis_index("zh") * lax.axis_size("zl") + lax.axis_index("zl")
    right = [(i, (i + 1) % nz) for i in range(nz)]
    left = [(i, (i - 1) % nz) for i in range(nz)]
    by_offset = {0: block}
    going_right, going_left = block, block
    for step in range(1, nz // 2 + 1):
        going_right = lax.ppermute(going_right, ("zh", "zl"), right)
        by_offset[-step] = going_right
        if step < nz - step:
            going_left = lax.ppermute(going_left, ("zh", "zl"), left)
            by_offset[step] = going_left
    lowest = -(nz // 2)
    relative = jnp.stack([by_offset[lowest + i] for i in range(nz)], 0)
    pick = (jnp.arange(nz, dtype=jnp.int32) - z - lowest) % nz
    return relative, pick


def block_body(tokens, in_weight, out_weight, short_taps, filter_taps, decay_rate, doc_lengths):
    zh = lax.axis_index("zh")
    col_size = lax.axis_size("zh") * lax.axis_size("zl") * lax.axis_size("c")
    own_rows = tokens.shape[0]
    col_rows = own_rows * col_size
    half = in_weight.shape[2] // 2
    tap_count = filter_taps.shape[0]

    widened = tokens.astype(jnp.float32)
    normed = (
        widened * lax.rsqrt(jnp.mean(widened * widened, axis=1, keepdims=True) + 1e-06)
    ).astype(jnp.bfloat16)
    in_piece = swap_half(in_weight, zh, 2)
    in_full = lax.all_gather(in_piece, "p", axis=0, tiled=True)
    gathered, pick = z_ring_gather(normed)

    chip_out = jnp.stack([out_weight, lax.ppermute(out_weight, "c", [(0, 1), (1, 0)])], 1)
    out_piece = swap_half(chip_out, zh, 2)
    out_full = lax.all_gather(out_piece, "p", axis=0, tiled=True)
    out_full = out_full.reshape(out_full.shape[0], 2 * half)

    flat_in = in_full.reshape(in_full.shape[0], 3 * half)
    nz = gathered.shape[0]

    def project(rows):
        flat = rows.reshape(nz * own_rows, rows.shape[2])
        out = jnp.dot(flat, flat_in, preferred_element_type=jnp.float32)
        return out.astype(jnp.bfloat16).reshape(nz, own_rows, 3 * half)

    partner_rows = lax.ppermute(gathered, "c", [(0, 1), (1, 0)])
    from_mine = project(gathered)
    from_partner = project(partner_rows)
    core = lax.axis_index("c")
    both = jnp.concatenate([from_mine, from_partner], 0)
    from_core = jnp.array([[0, 1]], jnp.int32) != core
    order = (from_core.astype(jnp.int32) * nz + pick[:, None]).reshape(2 * nz)
    projected = jnp.take(both, order, axis=0).reshape(col_rows, 3 * half)

    first_row = lax.axis_index("p") * col_rows
    wide_rows = tap_count + col_rows
    wide_points = first_row - tap_count + jnp.arange(wide_rows, dtype=jnp.int32)
    wide_position = doc_position(wide_points, doc_lengths)
    own_position = wide_position[tap_count:]

    columns = lax.axis_size("p")
    ahead = [(i, i + 1) for i in range(columns - 1)]
    my_taps = lax.dynamic_slice_in_dim(short_taps, zh * half, half, 2).reshape(3, 3 * half)
    my_filter = lax.dynamic_slice_in_dim(filter_taps, zh * half, half, 1)
    my_decay = lax.dynamic_slice_in_dim(decay_rate, zh * half, half, 0)

    before = lax.ppermute(projected[col_rows - tap_count - 2 :], "p", ahead)
    short_all = short_filter(
        jnp.concatenate([before, projected], 0), my_taps, wide_position, wide_rows
    )
    extended = lax.reduce_precision(
        short_all[:, half : 2 * half] * short_all[:, 2 * half :], exponent_bits=8, mantissa_bits=7
    )
    query = short_all[tap_count:, :half]
    shaped = my_filter * jnp.exp(
        -my_decay[None, :] * jnp.arange(tap_count, dtype=jnp.float32)[:, None]
    )
    long_mix = long_filter(extended, shaped, own_position, col_rows, tap_count)
    gated_mix = (query * long_mix).astype(jnp.bfloat16)
    gated_mix, out_full = lax.optimization_barrier((gated_mix, out_full))
    core = lax.axis_index("c")
    swap = [(0, 1), (1, 0)]
    by_core = gated_mix.reshape(nz, 2, own_rows, half)
    mine_rows = lax.dynamic_index_in_dim(by_core, core, 1, keepdims=False)
    other_rows = lax.dynamic_index_in_dim(by_core, 1 - core, 1, keepdims=False)
    partner_cols = lax.ppermute(other_rows, "c", swap)
    lhs = jnp.concatenate([mine_rows, partner_cols], 2).reshape(nz * own_rows, 2 * half)
    rhs = out_full
    summed = lax.psum_scatter(
        lax.dot_general(
            lhs, rhs, (((1,), (1,)), ((), ())), preferred_element_type=jnp.float32
        ).astype(jnp.bfloat16),
        ("zh", "zl"),
        scatter_dimension=0,
        tiled=True,
    ).astype(jnp.float32)
    return (widened + summed).astype(jnp.bfloat16)


def solution(mesh):
    fsdp, tp = mesh.shape["fsdp"], mesh.shape["tp"]
    grid = mesh.devices.reshape(fsdp // 2, 2, tp // 2, 2)
    fine = Mesh(grid, ("p", "zh", "zl", "c"))
    rows = ("p", "zh", "zl", "c")
    chan = ("zl", "c")
    in_specs = (
        P(rows, None),
        P(("p", "zh"), None, chan),
        P(("p", "zh"), chan),
        P(None, None, chan),
        P(None, chan),
        P(chan),
        P(),
    )
    out_specs = P(rows, None)
    return jax.shard_map(block_body, mesh=fine, in_specs=in_specs, out_specs=out_specs, check_vma=False)
```

```python
import jax
import jax.numpy as jnp
from jax import lax
from jax.sharding import Mesh
from jax.sharding import PartitionSpec as P


def doc_position(points, lengths):
    starts = jnp.cumsum(lengths) - lengths
    begins = jnp.max(jnp.where(starts[None, :] <= points[:, None], starts[None, :], 0), axis=1)
    return points - begins


def short_filter(extended, short_taps, positions, out_count):
    running = jnp.zeros((out_count,) + extended.shape[1:], jnp.float32)
    for tap_index in range(3):
        window = extended[2 - tap_index : 2 - tap_index + out_count].astype(jnp.float32)
        inside = (positions >= tap_index)[:, None]
        running = running + jnp.where(
            inside, short_taps[tap_index][None] * window, jnp.float32(0.0)
        )
    return running


def long_filter(extended, shaped, positions, out_count, tap_count, unroll=True):

    def tap_group(group_index, running):
        for inner in range(16):
            tap_index = group_index * 16 + inner
            window = lax.dynamic_slice_in_dim(extended, tap_count - tap_index, out_count, 0)
            weight_row = lax.dynamic_slice_in_dim(shaped, tap_index, 1, 0)
            inside = (positions >= tap_index)[:, None]
            running = running + jnp.where(
                inside, weight_row * window.astype(jnp.float32), jnp.float32(0.0)
            )
        return running

    zero_sum = jnp.zeros((out_count, shaped.shape[1]), jnp.float32)
    return lax.fori_loop(0, tap_count // 16, tap_group, zero_sum, unroll=unroll)


def swap_half(piece, zh, axis):
    width = piece.shape[axis] // 2
    lo = lax.slice_in_dim(piece, 0, width, axis=axis)
    hi = lax.slice_in_dim(piece, width, 2 * width, axis=axis)
    keep = jnp.where(zh == 0, lo, hi)
    give = jnp.where(zh == 0, hi, lo)
    got = lax.ppermute(give, "zh", [(0, 1), (1, 0)])
    first = jnp.where(zh == 0, keep, got)
    second = jnp.where(zh == 0, got, keep)
    return jnp.concatenate([first, second], 0)


def z_ring_gather(block):
    nz = lax.axis_size("zh") * lax.axis_size("zl")
    z = lax.axis_index("zh") * lax.axis_size("zl") + lax.axis_index("zl")
    right = [(i, (i + 1) % nz) for i in range(nz)]
    left = [(i, (i - 1) % nz) for i in range(nz)]
    by_offset = {0: block}
    going_right, going_left = block, block
    for step in range(1, nz // 2 + 1):
        going_right = lax.ppermute(going_right, ("zh", "zl"), right)
        by_offset[-step] = going_right
        if step < nz - step:
            going_left = lax.ppermute(going_left, ("zh", "zl"), left)
            by_offset[step] = going_left
    lowest = -(nz // 2)
    relative = jnp.stack([by_offset[lowest + i] for i in range(nz)], 0)
    pick = (jnp.arange(nz, dtype=jnp.int32) - z - lowest) % nz
    return relative, pick


def block_body(tokens, in_weight, out_weight, short_taps, filter_taps, decay_rate, doc_lengths):
    zh = lax.axis_index("zh")
    col_size = lax.axis_size("zh") * lax.axis_size("zl") * lax.axis_size("c")
    own_rows = tokens.shape[0]
    col_rows = own_rows * col_size
    half = in_weight.shape[2] // 2
    tap_count = filter_taps.shape[0]

    widened = tokens.astype(jnp.float32)
    normed = (
        widened * lax.rsqrt(jnp.mean(widened * widened, axis=1, keepdims=True) + 1e-06)
    ).astype(jnp.bfloat16)
    in_piece = swap_half(in_weight, zh, 2)
    in_full = lax.all_gather(in_piece, "p", axis=0, tiled=True)
    gathered, pick = z_ring_gather(normed)

    chip_out = jnp.stack([out_weight, lax.ppermute(out_weight, "c", [(0, 1), (1, 0)])], 1)
    out_piece = swap_half(chip_out, zh, 2)
    out_full = lax.all_gather(out_piece, "p", axis=0, tiled=True)
    out_full = out_full.reshape(out_full.shape[0], 2 * half)

    flat_in = in_full.reshape(in_full.shape[0], 3 * half)
    nz = gathered.shape[0]

    def project(rows):
        flat = rows.reshape(nz * own_rows, rows.shape[2])
        out = jnp.dot(flat, flat_in, preferred_element_type=jnp.float32)
        return out.astype(jnp.bfloat16).reshape(nz, own_rows, 3 * half)

    partner_rows = lax.ppermute(gathered, "c", [(0, 1), (1, 0)])
    from_mine = project(gathered)
    from_partner = project(partner_rows)
    core = lax.axis_index("c")
    both = jnp.concatenate([from_mine, from_partner], 0)
    from_core = jnp.array([[0, 1]], jnp.int32) != core
    order = (from_core.astype(jnp.int32) * nz + pick[:, None]).reshape(2 * nz)
    projected = jnp.take(both, order, axis=0).reshape(col_rows, 3 * half)

    first_row = lax.axis_index("p") * col_rows
    wide_rows = tap_count + col_rows
    wide_points = first_row - tap_count + jnp.arange(wide_rows, dtype=jnp.int32)
    wide_position = doc_position(wide_points, doc_lengths)
    own_position = wide_position[tap_count:]

    columns = lax.axis_size("p")
    ahead = [(i, i + 1) for i in range(columns - 1)]
    my_taps = lax.dynamic_slice_in_dim(short_taps, zh * half, half, 2).reshape(3, 3 * half)
    my_filter = lax.dynamic_slice_in_dim(filter_taps, zh * half, half, 1)
    my_decay = lax.dynamic_slice_in_dim(decay_rate, zh * half, half, 0)

    shaped = my_filter * jnp.exp(
        -my_decay[None, :] * jnp.arange(tap_count, dtype=jnp.float32)[:, None]
    )

    def kv_of(short_out):
        return lax.reduce_precision(
            short_out[:, half : 2 * half] * short_out[:, 2 * half :], exponent_bits=8, mantissa_bits=7
        )

    split = tap_count + 8
    before = lax.ppermute(projected[col_rows - tap_count - 2 :], "p", ahead)
    start = split - tap_count
    short_big = short_filter(
        projected[start - 2 :], my_taps, own_position[start:], col_rows - start
    )
    long_big = long_filter(
        kv_of(short_big), shaped, own_position[split:], col_rows - split, tap_count
    )
    query_big = short_big[tap_count:, :half]
    short_small = short_filter(
        jnp.concatenate([before, projected[:split]], 0),
        my_taps,
        wide_position[: tap_count + split],
        tap_count + split,
    )
    long_small = long_filter(
        kv_of(short_small), shaped, own_position[:split], split, tap_count, unroll=False
    )
    query_small = short_small[tap_count:, :half]
    gated_mix = jnp.concatenate(
        [query_small * long_small, query_big * long_big], 0
    ).astype(jnp.bfloat16)
    gated_mix, out_full = lax.optimization_barrier((gated_mix, out_full))
    core = lax.axis_index("c")
    swap = [(0, 1), (1, 0)]
    by_core = gated_mix.reshape(nz, 2, own_rows, half)
    mine_rows = lax.dynamic_index_in_dim(by_core, core, 1, keepdims=False)
    other_rows = lax.dynamic_index_in_dim(by_core, 1 - core, 1, keepdims=False)
    partner_cols = lax.ppermute(other_rows, "c", swap)
    lhs = jnp.concatenate([mine_rows, partner_cols], 2).reshape(nz * own_rows, 2 * half)
    rhs = out_full
    summed = lax.psum_scatter(
        lax.dot_general(
            lhs, rhs, (((1,), (1,)), ((), ())), preferred_element_type=jnp.float32
        ).astype(jnp.bfloat16),
        ("zh", "zl"),
        scatter_dimension=0,
        tiled=True,
    ).astype(jnp.float32)
    return (widened + summed).astype(jnp.bfloat16)


def solution(mesh):
    fsdp, tp = mesh.shape["fsdp"], mesh.shape["tp"]
    grid = mesh.devices.reshape(fsdp // 2, 2, tp // 2, 2)
    fine = Mesh(grid, ("p", "zh", "zl", "c"))
    rows = ("p", "zh", "zl", "c")
    chan = ("zl", "c")
    in_specs = (
        P(rows, None),
        P(("p", "zh"), None, chan),
        P(("p", "zh"), chan),
        P(None, None, chan),
        P(None, chan),
        P(chan),
        P(),
    )
    out_specs = P(rows, None)
    return jax.shard_map(block_body, mesh=fine, in_specs=in_specs, out_specs=out_specs, check_vma=False)
```

```python
import jax
import jax.numpy as jnp
from jax import lax
from jax.sharding import Mesh
from jax.sharding import PartitionSpec as P


def doc_position(points, lengths):
    starts = jnp.cumsum(lengths) - lengths
    begins = jnp.max(jnp.where(starts[None, :] <= points[:, None], starts[None, :], 0), axis=1)
    return points - begins


def short_filter(extended, short_taps, positions, out_count):
    running = jnp.zeros((out_count,) + extended.shape[1:], jnp.float32)
    for tap_index in range(3):
        window = extended[2 - tap_index : 2 - tap_index + out_count].astype(jnp.float32)
        inside = (positions >= tap_index)[:, None]
        running = running + jnp.where(
            inside, short_taps[tap_index][None] * window, jnp.float32(0.0)
        )
    return running


def long_filter(extended, shaped, positions, out_count, tap_count):

    def tap_group(group_index, running):
        for inner in range(16):
            tap_index = group_index * 16 + inner
            window = lax.dynamic_slice_in_dim(extended, tap_count - tap_index, out_count, 0)
            weight_row = lax.dynamic_slice_in_dim(shaped, tap_index, 1, 0)
            inside = (positions >= tap_index)[:, None]
            running = running + jnp.where(
                inside, weight_row * window.astype(jnp.float32), jnp.float32(0.0)
            )
        return running

    zero_sum = jnp.zeros((out_count, shaped.shape[1]), jnp.float32)
    return lax.fori_loop(0, tap_count // 16, tap_group, zero_sum, unroll=True)


def swap_half(piece, zh, axis):
    width = piece.shape[axis] // 2
    lo = lax.slice_in_dim(piece, 0, width, axis=axis)
    hi = lax.slice_in_dim(piece, width, 2 * width, axis=axis)
    keep = jnp.where(zh == 0, lo, hi)
    give = jnp.where(zh == 0, hi, lo)
    got = lax.ppermute(give, "zh", [(0, 1), (1, 0)])
    first = jnp.where(zh == 0, keep, got)
    second = jnp.where(zh == 0, got, keep)
    return jnp.concatenate([first, second], 0)


def z_ring_gather(block):
    nz = lax.axis_size("zh") * lax.axis_size("zl")
    z = lax.axis_index("zh") * lax.axis_size("zl") + lax.axis_index("zl")
    right = [(i, (i + 1) % nz) for i in range(nz)]
    left = [(i, (i - 1) % nz) for i in range(nz)]
    by_offset = {0: block}
    going_right, going_left = block, block
    for step in range(1, nz // 2 + 1):
        if step < nz - step:
            going_right = lax.ppermute(going_right, ("zh", "zl"), right)
            by_offset[-step] = going_right
            going_left = lax.ppermute(going_left, ("zh", "zl"), left)
            by_offset[step] = going_left
        else:
            cut = block.shape[0] // 2
            first = lax.ppermute(going_right[:cut], ("zh", "zl"), right)
            second = lax.ppermute(going_left[cut:], ("zh", "zl"), left)
            by_offset[-step] = jnp.concatenate([first, second], 0)
    lowest = -(nz // 2)
    relative = jnp.stack([by_offset[lowest + i] for i in range(nz)], 0)
    pick = (jnp.arange(nz, dtype=jnp.int32) - z - lowest) % nz
    return relative, pick


def block_body(tokens, in_weight, out_weight, short_taps, filter_taps, decay_rate, doc_lengths):
    zh = lax.axis_index("zh")
    col_size = lax.axis_size("zh") * lax.axis_size("zl") * lax.axis_size("c")
    own_rows = tokens.shape[0]
    col_rows = own_rows * col_size
    half = in_weight.shape[2] // 2
    tap_count = filter_taps.shape[0]

    widened = tokens.astype(jnp.float32)
    normed = (
        widened * lax.rsqrt(jnp.mean(widened * widened, axis=1, keepdims=True) + 1e-06)
    ).astype(jnp.bfloat16)
    in_piece = swap_half(in_weight, zh, 2)
    in_full = lax.all_gather(in_piece, "p", axis=0, tiled=True)
    gathered, pick = z_ring_gather(normed)

    chip_out = jnp.stack([out_weight, lax.ppermute(out_weight, "c", [(0, 1), (1, 0)])], 1)
    out_piece = swap_half(chip_out, zh, 2)
    out_full = lax.all_gather(out_piece, "p", axis=0, tiled=True)
    out_full = out_full.reshape(out_full.shape[0], 2 * half)

    flat_in = in_full.reshape(in_full.shape[0], 3 * half)
    nz = gathered.shape[0]

    def project(rows):
        flat = rows.reshape(nz * own_rows, rows.shape[2])
        out = jnp.dot(flat, flat_in, preferred_element_type=jnp.float32)
        return out.astype(jnp.bfloat16).reshape(nz, own_rows, 3 * half)

    partner_rows = lax.ppermute(gathered, "c", [(0, 1), (1, 0)])
    from_mine = project(gathered)
    from_partner = project(partner_rows)
    core = lax.axis_index("c")
    both = jnp.concatenate([from_mine, from_partner], 0)
    from_core = jnp.array([[0, 1]], jnp.int32) != core
    order = (from_core.astype(jnp.int32) * nz + pick[:, None]).reshape(2 * nz)
    projected = jnp.take(both, order, axis=0).reshape(col_rows, 3 * half)

    first_row = lax.axis_index("p") * col_rows
    wide_rows = tap_count + col_rows
    wide_points = first_row - tap_count + jnp.arange(wide_rows, dtype=jnp.int32)
    wide_position = doc_position(wide_points, doc_lengths)
    own_position = wide_position[tap_count:]

    columns = lax.axis_size("p")
    ahead = [(i, i + 1) for i in range(columns - 1)]
    my_taps = lax.dynamic_slice_in_dim(short_taps, zh * half, half, 2).reshape(3, 3 * half)
    my_filter = lax.dynamic_slice_in_dim(filter_taps, zh * half, half, 1)
    my_decay = lax.dynamic_slice_in_dim(decay_rate, zh * half, half, 0)

    before = lax.ppermute(projected[col_rows - tap_count - 2 :], "p", ahead)
    short_all = short_filter(
        jnp.concatenate([before, projected], 0), my_taps, wide_position, wide_rows
    )
    extended = lax.reduce_precision(
        short_all[:, half : 2 * half] * short_all[:, 2 * half :], exponent_bits=8, mantissa_bits=7
    )
    query = short_all[tap_count:, :half]
    shaped = my_filter * jnp.exp(
        -my_decay[None, :] * jnp.arange(tap_count, dtype=jnp.float32)[:, None]
    )
    long_mix = long_filter(extended, shaped, own_position, col_rows, tap_count)
    gated_mix = (query * long_mix).astype(jnp.bfloat16)
    gated_mix, out_full = lax.optimization_barrier((gated_mix, out_full))
    core = lax.axis_index("c")
    swap = [(0, 1), (1, 0)]
    by_core = gated_mix.reshape(nz, 2, own_rows, half)
    mine_rows = lax.dynamic_index_in_dim(by_core, core, 1, keepdims=False)
    other_rows = lax.dynamic_index_in_dim(by_core, 1 - core, 1, keepdims=False)
    partner_cols = lax.ppermute(other_rows, "c", swap)
    lhs = jnp.concatenate([mine_rows, partner_cols], 2).reshape(nz * own_rows, 2 * half)
    rhs = out_full
    summed = lax.psum_scatter(
        lax.dot_general(
            lhs, rhs, (((1,), (1,)), ((), ())), preferred_element_type=jnp.float32
        ).astype(jnp.bfloat16),
        ("zh", "zl"),
        scatter_dimension=0,
        tiled=True,
    ).astype(jnp.float32)
    return (widened + summed).astype(jnp.bfloat16)


def solution(mesh):
    fsdp, tp = mesh.shape["fsdp"], mesh.shape["tp"]
    grid = mesh.devices.reshape(fsdp // 2, 2, tp // 2, 2)
    fine = Mesh(grid, ("p", "zh", "zl", "c"))
    rows = ("p", "zh", "zl", "c")
    chan = ("zl", "c")
    in_specs = (
        P(rows, None),
        P(("p", "zh"), None, chan),
        P(("p", "zh"), chan),
        P(None, None, chan),
        P(None, chan),
        P(chan),
        P(),
    )
    out_specs = P(rows, None)
    return jax.shard_map(block_body, mesh=fine, in_specs=in_specs, out_specs=out_specs, check_vma=False)
```
